512 devices in a mesh: blk: 32 (over z, core), col: 16 (over y, x).
Axes of the slice: x: 4, y: 4, z: 16, core: 2. Of those that a mesh axis runs over, the one named last changes fastest.
Arguments:
- density: float32 [96, 7, 256, 256], P('blk', None, 'col'), as said below
- band_widths: int32 [96], P('blk'), may hold values from 1 to 3, as said below
Outputs:
- purified: float32 [96, 7, 256, 256], P('blk', None, 'col')
The draws below stay inside these ranges and needn't reach their ends.
Inputs may be any that keep to these rules, and one draw needn't show every extreme that they name: `band_widths`: each block row keeps between 1 and 3 blocks on each side; 3 is reached in every draw. `density`: diagonal entries of the diagonal blocks lie between 0.05 and 0.95, all other entries are small.
All inputs are finite; a program needn't handle non-finite values.
Results may differ from the reference program's by a relative error of at most 0.00013.
Values sent between devices are 32-bit elements; how exact they have to be, the bound alone decides.
No kernel may reach another device: no remote copies, remote signals or barrier semaphores. Data moves between devices by JAX's collectives and lax.ppermute only.
A program may use at most 64 MiB of HBM per device.

```python
import jax
import jax.numpy as jnp
from jax import lax

BS = 256
W = 3
NB = 96


def draw_density(key, part):
    shape = (NB, 2 * W + 1, BS, BS)
    first_key = jax.random.fold_in(key, 11)
    second_key = jax.random.fold_in(key, 12)
    noise = 0.007 * jax.random.normal(first_key, shape, jnp.float32)
    diagonal_values = jax.random.uniform(second_key, shape, jnp.float32, 0.15, 0.85)
    band_index = lax.broadcasted_iota(jnp.int32, shape, 1)
    column_index = lax.broadcasted_iota(jnp.int32, shape, 2)
    row_index = lax.broadcasted_iota(jnp.int32, shape, 3)
    on_diagonal = (band_index == W) & (column_index == row_index)
    return jnp.where(on_diagonal, diagonal_values, noise).astype(jnp.float32)


def draw_band_widths(key, part):
    drawn = jax.random.randint(jax.random.fold_in(key, 21), (NB,), 1, W + 1, dtype=jnp.int32)
    return drawn.at[0].set(W)


def setup_inputs(seed: int = 0) -> dict:
    key_of = jax.random.split(jax.random.key(seed), 3)
    return {
        "density": draw_density(jax.random.fold_in(key_of[2], 71), 0),
        "band_widths": draw_band_widths(jax.random.fold_in(key_of[2], 71), 0),
    }


def band_product(left, right):
    span = 2 * W + 1
    outputs = [None] * span
    for inner_band in range(span):
        shifted = jnp.roll(right, -(inner_band - W), axis=0)
        for right_band in range(span):
            source_band = right_band - inner_band + W
            if 0 <= source_band < span:
                term = jnp.einsum("irs,isc->irc", left[:, inner_band], shifted[:, source_band], precision=lax.Precision.HIGHEST)
                outputs[right_band] = term if outputs[right_band] is None else outputs[right_band] + term
    return jnp.stack(outputs, axis=1)


def reference(density, band_widths):
    offsets = jnp.abs(jnp.arange(2 * W + 1, dtype=jnp.int32) - W)
    pattern = (offsets[None, :] <= band_widths[:, None]).astype(jnp.float32)[:, :, None, None]
    current = jnp.swapaxes(density, 2, 3) * pattern
    for purify_step in range(2):
        square = band_product(current, current) * pattern
        third_power = band_product(current, square) * pattern
        current = 3.0 * square - 2.0 * third_power
    return jnp.swapaxes(current, 2, 3)
```

```python
import jax
import jax.numpy as jnp
from jax import lax
from jax.sharding import PartitionSpec as P

W = 3


def padded(cells, sides, width):
    for axis, dim in sides:
        count = lax.axis_size(axis)
        head = lax.slice_in_dim(cells, 0, width, axis=dim)
        tail = lax.slice_in_dim(cells, cells.shape[dim] - width, cells.shape[dim], axis=dim)
        cells = jnp.concatenate(
            [
                lax.ppermute(tail, axis, [(i, (i + 1) % count) for i in range(count)]),
                cells,
                lax.ppermute(head, axis, [((i + 1) % count, i) for i in range(count)]),
            ],
            axis=dim,
        )
    return cells


def extend(right):
    return padded(right, (("blk", 0),), W)


def contract(extended, shard_rows):
    local_rows = shard_rows.shape[0]
    summed_bands = [None] * (2 * W + 1)
    for inner_band in range(2 * W + 1):
        lowest = max(0, inner_band - W)
        highest = min(2 * W, inner_band + W)
        source_low = lowest - inner_band + W
        source_high = highest - inner_band + W
        block_terms = jnp.einsum(
            "ibcs,isr->ibcr",
            extended[inner_band : inner_band + local_rows, source_low : source_high + 1],
            shard_rows[:, inner_band],
            precision=lax.Precision.HIGHEST,
        )
        for right_band in range(lowest, highest + 1):
            term = block_terms[:, right_band - lowest]
            summed_bands[right_band] = (
                term if summed_bands[right_band] is None else summed_bands[right_band] + term
            )
    return jnp.stack(summed_bands, axis=1)


def gather_columns(cells):
    count = lax.axis_size("col")
    copies = jnp.tile(cells, (1, 1, count, 1))
    return lax.all_to_all(copies, "col", 2, 2, tiled=True)


def on_device(density, band_widths):
    offsets = jnp.abs(jnp.arange(2 * W + 1, dtype=jnp.int32) - W)
    pattern = (offsets[None, :] <= band_widths[:, None]).astype(jnp.float32)[:, :, None, None]
    current = density * pattern
    for purify_step in range(2):
        gathered = gather_columns(current)
        square = contract(extend(current), gathered) * pattern
        third_power = contract(extend(square), gathered) * pattern
        current = 3.0 * square - 2.0 * third_power
    return current


def solution(mesh):
    in_specs = (P("blk", None, "col", None), P("blk"))
    out_specs = P("blk", None, "col", None)
    return jax.shard_map(
        on_device, mesh=mesh, in_specs=in_specs, out_specs=out_specs, check_vma=False
    )
```

```python
import jax
import jax.numpy as jnp
from jax import lax
from jax.sharding import PartitionSpec as P

W = 3


def send(cells, shift):
    count = lax.axis_size("blk")
    return lax.ppermute(cells, "blk", [(i, (i + shift) % count) for i in range(count)])


def halo_pieces(cells):
    rows = cells.shape[0]
    tail = [cells[rows - W + k, W - k :] for k in range(W)]
    head = [cells[k, : 2 * W - k] for k in range(W)]
    return tail, head


def extend(right):
    tail, head = halo_pieces(right)
    from_left = send(jnp.concatenate(tail, axis=0), 1)
    from_right = send(jnp.concatenate(head, axis=0), -1)
    zero = jnp.zeros((1,) + right.shape[2:], right.dtype)
    rows = []
    start = 0
    for k in range(W):
        width = 2 * W + 1 - (W - k)
        piece = from_left[start : start + width]
        start += width
        rows.append(jnp.concatenate([jnp.broadcast_to(zero, (W - k,) + right.shape[2:]), piece], axis=0))
    left = jnp.stack(rows)
    rows = []
    start = 0
    for k in range(W):
        width = 2 * W - k
        piece = from_right[start : start + width]
        start += width
        rows.append(jnp.concatenate([piece, jnp.broadcast_to(zero, (k + 1,) + right.shape[2:])], axis=0))
    right_rows = jnp.stack(rows)
    return jnp.concatenate([left, right, right_rows], axis=0)


def contract(extended, shard_rows, pattern):
    local_rows = shard_rows.shape[0]
    summed_bands = [None] * (2 * W + 1)
    for inner_band in range(2 * W + 1):
        lowest = max(0, inner_band - W)
        highest = min(2 * W, inner_band + W)
        source_low = lowest - inner_band + W
        source_high = highest - inner_band + W
        block_terms = jnp.einsum(
            "ibcs,isr->ibcr",
            extended[inner_band : inner_band + local_rows, source_low : source_high + 1],
            shard_rows[:, inner_band] * pattern[:, inner_band],
            precision=lax.Precision.HIGHEST,
        )
        for right_band in range(lowest, highest + 1):
            term = block_terms[:, right_band - lowest]
            summed_bands[right_band] = (
                term if summed_bands[right_band] is None else summed_bands[right_band] + term
            )
    return jnp.stack(summed_bands, axis=1)


def on_device(density, band_widths):
    offsets = jnp.abs(jnp.arange(2 * W + 1, dtype=jnp.int32) - W)
    pattern = (offsets[None, :] <= band_widths[:, None]).astype(jnp.float32)[:, :, None, None]
    current = density * pattern
    for purify_step in range(2):
        source = density if purify_step == 0 else current
        gathered = lax.all_gather(source, "col", axis=2, tiled=True)
        square = contract(extend(current), gathered, pattern) * pattern
        third_power = contract(extend(square), gathered, pattern) * pattern
        current = 3.0 * square - 2.0 * third_power
    return current


def solution(mesh):
    in_specs = (P("blk", None, "col", None), P("blk"))
    out_specs = P("blk", None, "col", None)
    return jax.shard_map(
        on_device, mesh=mesh, in_specs=in_specs, out_specs=out_specs, check_vma=False
    )
```

```python
import jax
import jax.numpy as jnp
from jax import lax
from jax.sharding import PartitionSpec as P

W = 3


def send(cells, shift):
    count = lax.axis_size("blk")
    return lax.ppermute(cells, "blk", [(i, (i + shift) % count) for i in range(count)])


def halo_pieces(cells):
    rows = cells.shape[0]
    tail = [cells[rows - W + k, W - k :] for k in range(W)]
    head = [cells[k, : 2 * W - k] for k in range(W)]
    return tail, head


def extend(right):
    tail, head = halo_pieces(right)
    from_left = send(jnp.concatenate(tail, axis=0), 1)
    from_right = send(jnp.concatenate(head, axis=0), -1)
    zero = jnp.zeros((1,) + right.shape[2:], right.dtype)
    rows = []
    start = 0
    for k in range(W):
        width = 2 * W + 1 - (W - k)
        piece = from_left[start : start + width]
        start += width
        rows.append(jnp.concatenate([jnp.broadcast_to(zero, (W - k,) + right.shape[2:]), piece], axis=0))
    left = jnp.stack(rows)
    rows = []
    start = 0
    for k in range(W):
        width = 2 * W - k
        piece = from_right[start : start + width]
        start += width
        rows.append(jnp.concatenate([piece, jnp.broadcast_to(zero, (k + 1,) + right.shape[2:])], axis=0))
    right_rows = jnp.stack(rows)
    return jnp.concatenate([left, right, right_rows], axis=0)


def contract(extended, shard_rows):
    local_rows = shard_rows.shape[0]
    summed_bands = [None] * (2 * W + 1)
    for inner_band in range(2 * W + 1):
        lowest = max(0, inner_band - W)
        highest = min(2 * W, inner_band + W)
        source_low = lowest - inner_band + W
        source_high = highest - inner_band + W
        block_terms = jnp.einsum(
            "ibcs,isr->ibcr",
            extended[inner_band : inner_band + local_rows, source_low : source_high + 1],
            shard_rows[:, inner_band],
            precision=lax.Precision.HIGHEST,
        )
        for right_band in range(lowest, highest + 1):
            term = block_terms[:, right_band - lowest]
            summed_bands[right_band] = (
                term if summed_bands[right_band] is None else summed_bands[right_band] + term
            )
    return jnp.stack(summed_bands, axis=1)


def gather_columns(cells):
    count = lax.axis_size("col")
    copies = jnp.broadcast_to(cells[None], (count,) + cells.shape)
    pieces = lax.all_to_all(copies, "col", 0, 0, tiled=False)
    rows, bands, width, depth = cells.shape
    return jnp.moveaxis(pieces, 0, 2).reshape(rows, bands, count * width, depth)


def on_device(density, band_widths):
    offsets = jnp.abs(jnp.arange(2 * W + 1, dtype=jnp.int32) - W)
    pattern = (offsets[None, :] <= band_widths[:, None]).astype(jnp.float32)[:, :, None, None]
    current = density * pattern
    for purify_step in range(2):
        gathered = gather_columns(current)
        square = contract(extend(current), gathered) * pattern
        third_power = contract(extend(square), gathered) * pattern
        current = 3.0 * square - 2.0 * third_power
    return current


def solution(mesh):
    in_specs = (P("blk", None, "col", None), P("blk"))
    out_specs = P("blk", None, "col", None)
    return jax.shard_map(
        on_device, mesh=mesh, in_specs=in_specs, out_specs=out_specs, check_vma=False
    )
```

```python
import jax
import jax.numpy as jnp
from jax import lax
from jax.experimental import pallas as pl
from jax.sharding import PartitionSpec as P

W = 3


def send(cells, shift):
    count = lax.axis_size("blk")
    return lax.ppermute(cells, "blk", [(i, (i + shift) % count) for i in range(count)])


def halo_pieces(cells):
    rows = cells.shape[0]
    tail = [cells[rows - W + k, W - k :] for k in range(W)]
    head = [cells[k, : 2 * W - k] for k in range(W)]
    return tail, head


def extend(right):
    tail, head = halo_pieces(right)
    from_left = send(jnp.concatenate(tail, axis=0), 1)
    from_right = send(jnp.concatenate(head, axis=0), -1)
    zero = jnp.zeros((1,) + right.shape[2:], right.dtype)
    rows = []
    start = 0
    for k in range(W):
        width = 2 * W + 1 - (W - k)
        piece = from_left[start : start + width]
        start += width
        rows.append(jnp.concatenate([jnp.broadcast_to(zero, (W - k,) + right.shape[2:]), piece], axis=0))
    left = jnp.stack(rows)
    rows = []
    start = 0
    for k in range(W):
        width = 2 * W - k
        piece = from_right[start : start + width]
        start += width
        rows.append(jnp.concatenate([piece, jnp.broadcast_to(zero, (k + 1,) + right.shape[2:])], axis=0))
    right_rows = jnp.stack(rows)
    return jnp.concatenate([left, right, right_rows], axis=0)


def band_kernel(ext_ref, left_ref, out_ref):
    rows = out_ref.shape[0]
    width = out_ref.shape[2]
    for i in range(rows):
        summed = [None] * (2 * W + 1)
        for a in range(2 * W + 1):
            lo, hi = max(0, a - W), min(2 * W, a + W)
            count = hi - lo + 1
            lhs = ext_ref[i + a, lo - a + W : hi - a + W + 1].reshape(count * width, -1)
            res = jnp.dot(lhs, left_ref[i, a], precision=lax.Precision.HIGHEST, preferred_element_type=jnp.float32)
            for b in range(lo, hi + 1):
                part = res[(b - lo) * width : (b - lo + 1) * width]
                summed[b] = part if summed[b] is None else summed[b] + part
        for b in range(2 * W + 1):
            out_ref[i, b] = summed[b]
def contract_kernel(extended, shard_rows):
    rows, bands, width, depth = extended.shape[0] - 2 * W, extended.shape[1], extended.shape[2], extended.shape[3]
    flops = 2 * rows * 37 * width * depth * shard_rows.shape[2]
    nbytes = 4 * (extended.size + shard_rows.size + rows * bands * width * depth)
    return pl.pallas_call(band_kernel, out_shape=jax.ShapeDtypeStruct((rows, bands, width, depth), jnp.float32),
        cost_estimate=pl.CostEstimate(flops=flops, transcendentals=0, bytes_accessed=nbytes))(extended, shard_rows)


def on_device(density, band_widths):
    offsets = jnp.abs(jnp.arange(2 * W + 1, dtype=jnp.int32) - W)
    pattern = (offsets[None, :] <= band_widths[:, None]).astype(jnp.float32)[:, :, None, None]
    current = density * pattern
    for purify_step in range(2):
        gathered = lax.all_gather(current, "col", axis=2, tiled=True)
        square = contract_kernel(extend(current), gathered) * pattern
        third_power = contract_kernel(extend(square), gathered) * pattern
        current = 3.0 * square - 2.0 * third_power
    return current


def solution(mesh):
    in_specs = (P("blk", None, "col", None), P("blk"))
    out_specs = P("blk", None, "col", None)
    return jax.shard_map(
        on_device, mesh=mesh, in_specs=in_specs, out_specs=out_specs, check_vma=False
    )
```

```python
import functools

import jax
import jax.numpy as jnp
from jax import lax
from jax.experimental import pallas as pl
from jax.experimental.pallas import tpu as pltpu
from jax.sharding import PartitionSpec as P

W = 3


def send(cells, shift):
    count = lax.axis_size("blk")
    return lax.ppermute(cells, "blk", [(i, (i + shift) % count) for i in range(count)])


def halo_pieces(cells):
    rows = cells.shape[0]
    tail = [cells[rows - W + k, W - k :] for k in range(W)]
    head = [cells[k, : 2 * W - k] for k in range(W)]
    return tail, head


def extend(right):
    tail, head = halo_pieces(right)
    from_left = send(jnp.concatenate(tail, axis=0), 1)
    from_right = send(jnp.concatenate(head, axis=0), -1)
    zero = jnp.zeros((1,) + right.shape[2:], right.dtype)
    rows = []
    start = 0
    for k in range(W):
        width = 2 * W + 1 - (W - k)
        piece = from_left[start : start + width]
        start += width
        rows.append(jnp.concatenate([jnp.broadcast_to(zero, (W - k,) + right.shape[2:]), piece], axis=0))
    left = jnp.stack(rows)
    rows = []
    start = 0
    for k in range(W):
        width = 2 * W - k
        piece = from_right[start : start + width]
        start += width
        rows.append(jnp.concatenate([piece, jnp.broadcast_to(zero, (k + 1,) + right.shape[2:])], axis=0))
    right_rows = jnp.stack(rows)
    return jnp.concatenate([left, right, right_rows], axis=0)


def band_kernel(ext_ref, left_ref, keep_ref, out_ref, *, combine):
    rows = out_ref.shape[0]
    width = out_ref.shape[2]
    for i in range(rows):
        summed = [None] * (2 * W + 1)
        for a in range(2 * W + 1):
            lo, hi = max(0, a - W), min(2 * W, a + W)
            count = hi - lo + 1
            lhs = ext_ref[i + a, lo - a + W : hi - a + W + 1].reshape(count * width, -1)
            res = jnp.dot(lhs, left_ref[i, a], precision=lax.Precision.HIGHEST, preferred_element_type=jnp.float32)
            for b in range(lo, hi + 1):
                part = res[(b - lo) * width : (b - lo + 1) * width]
                summed[b] = part if summed[b] is None else summed[b] + part
        for b in range(2 * W + 1):
            masked = summed[b] * keep_ref[i, b]
            if combine:
                masked = 3.0 * ext_ref[W + i, b] - 2.0 * masked
            out_ref[i, b] = masked


def contract_kernel(extended, shard_rows, keep, combine):
    rows, bands, width, depth = extended.shape[0] - 2 * W, extended.shape[1], extended.shape[2], extended.shape[3]
    flops = 2 * rows * 37 * width * depth * shard_rows.shape[2]
    nbytes = 4 * (extended.size + shard_rows.size + rows * bands * width * depth)
    vmem = pl.BlockSpec(memory_space=pltpu.VMEM)
    return pl.pallas_call(
        functools.partial(band_kernel, combine=combine),
        out_shape=jax.ShapeDtypeStruct((rows, bands, width, depth), jnp.float32),
        in_specs=[vmem, vmem, pl.BlockSpec(memory_space=pltpu.SMEM)],
        out_specs=vmem,
        cost_estimate=pl.CostEstimate(flops=flops, transcendentals=0, bytes_accessed=nbytes),
    )(extended, shard_rows, keep)


def on_device(density, band_widths):
    offsets = jnp.abs(jnp.arange(2 * W + 1, dtype=jnp.int32) - W)
    pattern = (offsets[None, :] <= band_widths[:, None]).astype(jnp.float32)[:, :, None, None]
    current = density * pattern
    keep = pattern[:, :, 0, 0]
    for purify_step in range(2):
        gathered = lax.all_gather(current, "col", axis=2, tiled=True)
        square = contract_kernel(extend(current), gathered, keep, False)
        current = contract_kernel(extend(square), gathered, keep, True)
    return current


def solution(mesh):
    in_specs = (P("blk", None, "col", None), P("blk"))
    out_specs = P("blk", None, "col", None)
    return jax.shard_map(
        on_device, mesh=mesh, in_specs=in_specs, out_specs=out_specs, check_vma=False
    )
```

```python
import jax
import jax.numpy as jnp
from jax import lax
from jax.sharding import PartitionSpec as P

W = 3


def padded(cells, sides, width):
    for axis, dim in sides:
        count = lax.axis_size(axis)
        head = lax.slice_in_dim(cells, 0, width, axis=dim)
        tail = lax.slice_in_dim(cells, cells.shape[dim] - width, cells.shape[dim], axis=dim)
        cells = jnp.concatenate(
            [
                lax.ppermute(tail, axis, [(i, (i + 1) % count) for i in range(count)]),
                cells,
                lax.ppermute(head, axis, [((i + 1) % count, i) for i in range(count)]),
            ],
            axis=dim,
        )
    return cells


def extend(right):
    return padded(right, (("blk", 0),), W)


def contract(extended, shard_rows):
    local_rows = shard_rows.shape[0]
    span = 2 * W + 1
    zeros = jnp.zeros_like(extended[:local_rows, :1])
    shifted = []
    for inner_band in range(span):
        window = extended[inner_band : inner_band + local_rows]
        shift = inner_band - W
        if shift > 0:
            window = jnp.concatenate([zeros] * shift + [window[:, : span - shift]], axis=1)
        elif shift < 0:
            window = jnp.concatenate([window[:, -shift:]] + [zeros] * (-shift), axis=1)
        shifted.append(window)
    stacked = jnp.stack(shifted, axis=3)
    return jnp.einsum("ibcas,iasr->ibcr", stacked, shard_rows, precision=lax.Precision.HIGHEST)


def on_device(density, band_widths):
    offsets = jnp.abs(jnp.arange(2 * W + 1, dtype=jnp.int32) - W)
    pattern = (offsets[None, :] <= band_widths[:, None]).astype(jnp.float32)[:, :, None, None]
    current = density * pattern
    for purify_step in range(2):
        gathered = lax.all_gather(current, "col", axis=2, tiled=True)
        square = contract(extend(current), gathered) * pattern
        third_power = contract(extend(square), gathered) * pattern
        current = 3.0 * square - 2.0 * third_power
    return current


def solution(mesh):
    in_specs = (P("blk", None, "col", None), P("blk"))
    out_specs = P("blk", None, "col", None)
    return jax.shard_map(
        on_device, mesh=mesh, in_specs=in_specs, out_specs=out_specs, check_vma=False
    )
```

```python
import jax
import jax.numpy as jnp
from jax import lax
from jax.sharding import PartitionSpec as P

W = 3


def send(cells, shift):
    count = lax.axis_size("blk")
    return lax.ppermute(cells, "blk", [(i, (i + shift) % count) for i in range(count)])


def halo_pieces(cells):
    rows = cells.shape[0]
    tail = [cells[rows - W + k, W - k :] for k in range(W)]
    head = [cells[k, : 2 * W - k] for k in range(W)]
    return tail, head


def extend(right):
    tail, head = halo_pieces(right)
    from_left = send(jnp.concatenate(tail, axis=0), 1)
    from_right = send(jnp.concatenate(head, axis=0), -1)
    zero = jnp.zeros((1,) + right.shape[2:], right.dtype)
    rows = []
    start = 0
    for k in range(W):
        width = 2 * W + 1 - (W - k)
        piece = from_left[start : start + width]
        start += width
        rows.append(jnp.concatenate([jnp.broadcast_to(zero, (W - k,) + right.shape[2:]), piece], axis=0))
    left = jnp.stack(rows)
    rows = []
    start = 0
    for k in range(W):
        width = 2 * W - k
        piece = from_right[start : start + width]
        start += width
        rows.append(jnp.concatenate([piece, jnp.broadcast_to(zero, (k + 1,) + right.shape[2:])], axis=0))
    right_rows = jnp.stack(rows)
    return jnp.concatenate([left, right, right_rows], axis=0)


def contract(extended, shard_rows):
    local_rows = shard_rows.shape[0]
    span = 2 * W + 1
    zeros = jnp.zeros_like(extended[:local_rows, :1])
    shifted = []
    for inner_band in range(span):
        window = extended[inner_band : inner_band + local_rows]
        shift = inner_band - W
        if shift > 0:
            window = jnp.concatenate([zeros] * shift + [window[:, : span - shift]], axis=1)
        elif shift < 0:
            window = jnp.concatenate([window[:, -shift:]] + [zeros] * (-shift), axis=1)
        shifted.append(window)
    stacked = jnp.stack(shifted, axis=3)
    return jnp.einsum("ibcas,iasr->ibcr", stacked, shard_rows, precision=lax.Precision.HIGHEST)


def on_device(density, band_widths):
    offsets = jnp.abs(jnp.arange(2 * W + 1, dtype=jnp.int32) - W)
    pattern = (offsets[None, :] <= band_widths[:, None]).astype(jnp.float32)[:, :, None, None]
    current = density * pattern
    for purify_step in range(2):
        gathered = lax.all_gather(current, "col", axis=2, tiled=True)
        square = contract(extend(current), gathered) * pattern
        third_power = contract(extend(square), gathered) * pattern
        current = 3.0 * square - 2.0 * third_power
    return current


def solution(mesh):
    in_specs = (P("blk", None, "col", None), P("blk"))
    out_specs = P("blk", None, "col", None)
    return jax.shard_map(
        on_device, mesh=mesh, in_specs=in_specs, out_specs=out_specs, check_vma=False
    )
```

```python
import jax
import jax.numpy as jnp
from jax import lax
from jax.sharding import PartitionSpec as P

W = 3


def send(cells, shift):
    count = lax.axis_size("blk")
    return lax.ppermute(cells, "blk", [(i, (i + shift) % count) for i in range(count)])


def halo_pieces(cells):
    rows = cells.shape[0]
    tail = [cells[rows - W + k, W - k :] for k in range(W)]
    head = [cells[k, : 2 * W - k] for k in range(W)]
    return tail, head


def extend(right):
    tail, head = halo_pieces(right)
    from_left = send(jnp.concatenate(tail, axis=0), 1)
    from_right = send(jnp.concatenate(head, axis=0), -1)
    zero = jnp.zeros((1,) + right.shape[2:], right.dtype)
    rows = []
    start = 0
    for k in range(W):
        width = 2 * W + 1 - (W - k)
        piece = from_left[start : start + width]
        start += width
        rows.append(jnp.concatenate([jnp.broadcast_to(zero, (W - k,) + right.shape[2:]), piece], axis=0))
    left = jnp.stack(rows)
    rows = []
    start = 0
    for k in range(W):
        width = 2 * W - k
        piece = from_right[start : start + width]
        start += width
        rows.append(jnp.concatenate([piece, jnp.broadcast_to(zero, (k + 1,) + right.shape[2:])], axis=0))
    right_rows = jnp.stack(rows)
    return jnp.concatenate([left, right, right_rows], axis=0)


def contract(extended, shard_rows):
    local_rows = shard_rows.shape[0]
    span = 2 * W + 1
    zeros = jnp.zeros_like(extended[:local_rows, :1])
    shifted = []
    for inner_band in range(span):
        window = extended[inner_band : inner_band + local_rows]
        shift = inner_band - W
        if shift > 0:
            window = jnp.concatenate([zeros] * shift + [window[:, : span - shift]], axis=1)
        elif shift < 0:
            window = jnp.concatenate([window[:, -shift:]] + [zeros] * (-shift), axis=1)
        shifted.append(window)
    stacked = jnp.stack(shifted, axis=3)
    return jnp.einsum("ibcas,iasr->ibcr", stacked, shard_rows, precision=lax.Precision.HIGH)


def on_device(density, band_widths):
    offsets = jnp.abs(jnp.arange(2 * W + 1, dtype=jnp.int32) - W)
    pattern = (offsets[None, :] <= band_widths[:, None]).astype(jnp.float32)[:, :, None, None]
    current = density * pattern
    for purify_step in range(2):
        gathered = lax.all_gather(current, "col", axis=2, tiled=True)
        square = contract(extend(current), gathered) * pattern
        third_power = contract(extend(square), gathered) * pattern
        current = 3.0 * square - 2.0 * third_power
    return current


def solution(mesh):
    in_specs = (P("blk", None, "col", None), P("blk"))
    out_specs = P("blk", None, "col", None)
    return jax.shard_map(
        on_device, mesh=mesh, in_specs=in_specs, out_specs=out_specs, check_vma=False
    )
```

```python
import jax
import jax.numpy as jnp
from jax import lax
from jax.sharding import PartitionSpec as P

W = 3


def send(cells, shift):
    count = lax.axis_size("blk")
    return lax.ppermute(cells, "blk", [(i, (i + shift) % count) for i in range(count)])


def halo_pieces(cells):
    rows = cells.shape[0]
    tail = [cells[rows - W + k, W - k :] for k in range(W)]
    head = [cells[k, : 2 * W - k] for k in range(W)]
    return tail, head


def extend(right):
    tail, head = halo_pieces(right)
    from_left = send(jnp.concatenate(tail, axis=0), 1)
    from_right = send(jnp.concatenate(head, axis=0), -1)
    zero = jnp.zeros((1,) + right.shape[2:], right.dtype)
    rows = []
    start = 0
    for k in range(W):
        width = 2 * W + 1 - (W - k)
        piece = from_left[start : start + width]
        start += width
        rows.append(jnp.concatenate([jnp.broadcast_to(zero, (W - k,) + right.shape[2:]), piece], axis=0))
    left = jnp.stack(rows)
    rows = []
    start = 0
    for k in range(W):
        width = 2 * W - k
        piece = from_right[start : start + width]
        start += width
        rows.append(jnp.concatenate([piece, jnp.broadcast_to(zero, (k + 1,) + right.shape[2:])], axis=0))
    right_rows = jnp.stack(rows)
    return jnp.concatenate([left, right, right_rows], axis=0)


def contract(extended, shard_rows, keep=None):
    local_rows = shard_rows.shape[0]
    span = 2 * W + 1
    zeros = jnp.zeros_like(extended[:local_rows, :1])
    shifted = []
    for inner_band in range(span):
        window = extended[inner_band : inner_band + local_rows]
        shift = inner_band - W
        if shift > 0:
            window = jnp.concatenate([zeros] * shift + [window[:, : span - shift]], axis=1)
        elif shift < 0:
            window = jnp.concatenate([window[:, -shift:]] + [zeros] * (-shift), axis=1)
        shifted.append(window)
    stacked = jnp.stack(shifted, axis=3)
    if keep is not None:
        shard_rows = shard_rows * keep
    return jnp.einsum("ibcas,iasr->ibcr", stacked, shard_rows, precision=lax.Precision.HIGH)


def on_device(density, band_widths):
    offsets = jnp.abs(jnp.arange(2 * W + 1, dtype=jnp.int32) - W)
    pattern = (offsets[None, :] <= band_widths[:, None]).astype(jnp.float32)[:, :, None, None]
    current = density * pattern
    for purify_step in range(2):
        if purify_step == 0:
            gathered, keep = lax.all_gather(density, "col", axis=2, tiled=True), pattern
        else:
            gathered, keep = lax.all_gather(current, "col", axis=2, tiled=True), None
        square = contract(extend(current), gathered, keep) * pattern
        third_power = contract(extend(square), gathered, keep) * pattern
        current = 3.0 * square - 2.0 * third_power
    return current


def solution(mesh):
    in_specs = (P("blk", None, "col", None), P("blk"))
    out_specs = P("blk", None, "col", None)
    return jax.shard_map(
        on_device, mesh=mesh, in_specs=in_specs, out_specs=out_specs, check_vma=False
    )
```

```python
import jax
import jax.numpy as jnp
from jax import lax
from jax.sharding import PartitionSpec as P

W = 3


def send(cells, shift):
    count = lax.axis_size("blk")
    return lax.ppermute(cells, "blk", [(i, (i + shift) % count) for i in range(count)])


def halo_pieces(cells):
    rows = cells.shape[0]
    tail = [cells[rows - W + k, W - k :] for k in range(W)]
    head = [cells[k, : 2 * W - k] for k in range(W)]
    return tail, head


def extend(right):
    tail, head = halo_pieces(right)
    tail = jnp.concatenate(tail, axis=0)
    head = jnp.concatenate(head, axis=0)
    count = lax.axis_size("blk")
    odd = lax.axis_index("blk") % 2 == 1
    across = lax.ppermute(
        jnp.where(odd, tail, head),
        "blk",
        [(i, (i + 1) % count) if i % 2 else (i, (i - 1) % count) for i in range(count)],
    )
    within = lax.ppermute(
        jnp.where(odd, head, tail),
        "blk",
        [(i, i - 1) if i % 2 else (i, i + 1) for i in range(count)],
    )
    from_left = jnp.where(odd, within, across)
    from_right = jnp.where(odd, across, within)
    zero = jnp.zeros((1,) + right.shape[2:], right.dtype)
    rows = []
    start = 0
    for k in range(W):
        width = 2 * W + 1 - (W - k)
        piece = from_left[start : start + width]
        start += width
        rows.append(jnp.concatenate([jnp.broadcast_to(zero, (W - k,) + right.shape[2:]), piece], axis=0))
    left = jnp.stack(rows)
    rows = []
    start = 0
    for k in range(W):
        width = 2 * W - k
        piece = from_right[start : start + width]
        start += width
        rows.append(jnp.concatenate([piece, jnp.broadcast_to(zero, (k + 1,) + right.shape[2:])], axis=0))
    right_rows = jnp.stack(rows)
    return jnp.concatenate([left, right, right_rows], axis=0)


def contract(extended, shard_rows, keep=None):
    local_rows = shard_rows.shape[0]
    span = 2 * W + 1
    zeros = jnp.zeros_like(extended[:local_rows, :1])
    shifted = []
    for inner_band in range(span):
        window = extended[inner_band : inner_band + local_rows]
        shift = inner_band - W
        if shift > 0:
            window = jnp.concatenate([zeros] * shift + [window[:, : span - shift]], axis=1)
        elif shift < 0:
            window = jnp.concatenate([window[:, -shift:]] + [zeros] * (-shift), axis=1)
        shifted.append(window)
    stacked = jnp.stack(shifted, axis=3)
    if keep is not None:
        shard_rows = shard_rows * keep
    return jnp.einsum("ibcas,iasr->ibcr", stacked, shard_rows, precision=lax.Precision.HIGH)


def on_device(density, band_widths):
    offsets = jnp.abs(jnp.arange(2 * W + 1, dtype=jnp.int32) - W)
    pattern = (offsets[None, :] <= band_widths[:, None]).astype(jnp.float32)[:, :, None, None]
    current = density * pattern
    for purify_step in range(2):
        if purify_step == 0:
            gathered, keep = lax.all_gather(density, "col", axis=2, tiled=True), pattern
        else:
            gathered, keep = lax.all_gather(current, "col", axis=2, tiled=True), None
        square = contract(extend(current), gathered, keep) * pattern
        third_power = contract(extend(square), gathered, keep) * pattern
        current = 3.0 * square - 2.0 * third_power
    return current


def solution(mesh):
    in_specs = (P("blk", None, "col", None), P("blk"))
    out_specs = P("blk", None, "col", None)
    return jax.shard_map(
        on_device, mesh=mesh, in_specs=in_specs, out_specs=out_specs, check_vma=False
    )
```

```python
import jax
import jax.numpy as jnp
from jax import lax
from jax.sharding import PartitionSpec as P

W = 3


def send(cells, shift):
    count = lax.axis_size("blk")
    return lax.ppermute(cells, "blk", [(i, (i + shift) % count) for i in range(count)])


def halo_pieces(cells):
    rows = cells.shape[0]
    tail = [cells[rows - W + k, W - k :] for k in range(W)]
    head = [cells[k, : 2 * W - k] for k in range(W)]
    return tail, head


def extend(right):
    tail, head = halo_pieces(right)
    from_left = send(jnp.concatenate(tail, axis=0), 1)
    from_right = send(jnp.concatenate(head, axis=0), -1)
    zero = jnp.zeros((1,) + right.shape[2:], right.dtype)
    rows = []
    start = 0
    for k in range(W):
        width = 2 * W + 1 - (W - k)
        piece = from_left[start : start + width]
        start += width
        rows.append(jnp.concatenate([jnp.broadcast_to(zero, (W - k,) + right.shape[2:]), piece], axis=0))
    left = jnp.stack(rows)
    rows = []
    start = 0
    for k in range(W):
        width = 2 * W - k
        piece = from_right[start : start + width]
        start += width
        rows.append(jnp.concatenate([piece, jnp.broadcast_to(zero, (k + 1,) + right.shape[2:])], axis=0))
    right_rows = jnp.stack(rows)
    return jnp.concatenate([left, right, right_rows], axis=0)


def contract(extended, shard_rows, keep=None, scale=None):
    local_rows = shard_rows.shape[0]
    span = 2 * W + 1
    zeros = jnp.zeros_like(extended[:local_rows, :1])
    shifted = []
    for inner_band in range(span):
        window = extended[inner_band : inner_band + local_rows]
        shift = inner_band - W
        if shift > 0:
            window = jnp.concatenate([zeros] * shift + [window[:, : span - shift]], axis=1)
        elif shift < 0:
            window = jnp.concatenate([window[:, -shift:]] + [zeros] * (-shift), axis=1)
        shifted.append(window)
    stacked = jnp.stack(shifted, axis=3)
    if scale is not None:
        stacked = stacked * scale[:, :, :, None]
    if keep is not None:
        shard_rows = shard_rows * keep
    return jnp.einsum("ibcas,iasr->ibcr", stacked, shard_rows, precision=lax.Precision.HIGH)


def on_device(density, band_widths):
    offsets = jnp.abs(jnp.arange(2 * W + 1, dtype=jnp.int32) - W)
    pattern = (offsets[None, :] <= band_widths[:, None]).astype(jnp.float32)[:, :, None, None]
    current = density * pattern
    for purify_step in range(2):
        if purify_step == 0:
            gathered, keep = lax.all_gather(density, "col", axis=2, tiled=True), pattern
        else:
            gathered, keep = lax.all_gather(current, "col", axis=2, tiled=True), None
        square = contract(extend(current), gathered, keep) * pattern
        scaled_third = contract(extend(square), gathered, keep, -2.0 * pattern)
        current = 3.0 * square + scaled_third
    return current


def solution(mesh):
    in_specs = (P("blk", None, "col", None), P("blk"))
    out_specs = P("blk", None, "col", None)
    return jax.shard_map(
        on_device, mesh=mesh, in_specs=in_specs, out_specs=out_specs, check_vma=False
    )
```

```python
import jax
import jax.numpy as jnp
from jax import lax
from jax.sharding import PartitionSpec as P

W = 3


def send(cells, shift):
    count = lax.axis_size("blk")
    return lax.ppermute(cells, "blk", [(i, (i + shift) % count) for i in range(count)])


def halo_pieces(cells):
    rows = cells.shape[0]
    tail = [cells[rows - W + k, W - k :] for k in range(W)]
    head = [cells[k, : 2 * W - k] for k in range(W)]
    return tail, head


def extend(right):
    tail, head = halo_pieces(right)
    from_left = send(jnp.concatenate(tail, axis=0), 1)
    from_right = send(jnp.concatenate(head, axis=0), -1)
    zero = jnp.zeros((1,) + right.shape[2:], right.dtype)
    rows = []
    start = 0
    for k in range(W):
        width = 2 * W + 1 - (W - k)
        piece = from_left[start : start + width]
        start += width
        rows.append(jnp.concatenate([jnp.broadcast_to(zero, (W - k,) + right.shape[2:]), piece], axis=0))
    left = jnp.stack(rows)
    rows = []
    start = 0
    for k in range(W):
        width = 2 * W - k
        piece = from_right[start : start + width]
        start += width
        rows.append(jnp.concatenate([piece, jnp.broadcast_to(zero, (k + 1,) + right.shape[2:])], axis=0))
    right_rows = jnp.stack(rows)
    return jnp.concatenate([left, right, right_rows], axis=0)


def contract(extended, shard_rows, keep=None):
    local_rows = shard_rows.shape[0]
    span = 2 * W + 1
    if keep is not None:
        shard_rows = shard_rows * keep
    zeros = jnp.zeros_like(extended[:local_rows, :1])
    total = None
    for first, last in ((0, W - 2), (W - 1, W + 1), (W + 2, 2 * W)):
        out_low = max(0, first - W)
        out_high = min(2 * W, last + W)
        shifted = []
        for inner_band in range(first, last + 1):
            window = extended[inner_band : inner_band + local_rows]
            low = out_low - inner_band + W
            high = out_high - inner_band + W
            pieces = [zeros] * max(0, -low) + [window[:, max(0, low) : min(span, high + 1)]]
            pieces += [zeros] * max(0, high - (span - 1))
            shifted.append(jnp.concatenate(pieces, axis=1) if len(pieces) > 1 else pieces[0])
        stacked = jnp.stack(shifted, axis=3)
        part = jnp.einsum(
            "ibcas,iasr->ibcr",
            stacked,
            shard_rows[:, first : last + 1],
            precision=lax.Precision.HIGH,
        )
        part = jnp.pad(part, ((0, 0), (out_low, 2 * W - out_high), (0, 0), (0, 0)))
        total = part if total is None else total + part
    return total


def on_device(density, band_widths):
    offsets = jnp.abs(jnp.arange(2 * W + 1, dtype=jnp.int32) - W)
    pattern = (offsets[None, :] <= band_widths[:, None]).astype(jnp.float32)[:, :, None, None]
    current = density * pattern
    for purify_step in range(2):
        if purify_step == 0:
            gathered, keep = lax.all_gather(density, "col", axis=2, tiled=True), pattern
        else:
            gathered, keep = lax.all_gather(current, "col", axis=2, tiled=True), None
        square = contract(extend(current), gathered, keep) * pattern
        third_power = contract(extend(square), gathered, keep) * pattern
        current = 3.0 * square - 2.0 * third_power
    return current


def solution(mesh):
    in_specs = (P("blk", None, "col", None), P("blk"))
    out_specs = P("blk", None, "col", None)
    return jax.shard_map(
        on_device, mesh=mesh, in_specs=in_specs, out_specs=out_specs, check_vma=False
    )
```
